512 devices in a mesh: seg: 16 (over z), exp: 32 (over y, x, core).
Axes of the slice: x: 4, y: 4, z: 16, core: 2. Of those that a mesh axis runs over, the one named last changes fastest.
Arguments:
- queries: bfloat16 [16384, 8192], P('seg', 'exp'), may hold values from -6 to 6
- keys: bfloat16 [16384, 8192], P('seg', 'exp'), may hold values from -0.52734375 to 0.52734375
- values: bfloat16 [16384, 8192], P('seg', 'exp'), may hold values from -2000 to 2000
- log_decay: float32 [64, 16384], P('exp', 'seg'), may hold values from -1 to 0
- gain: float32 [8192], P('exp'), may hold values from 0.5 to 1.5
- d_out: bfloat16 [16384, 8192], P('seg', 'exp'), may hold values from -6 to 6
Outputs:
- out: bfloat16 [16384, 8192], P('seg', 'exp')
- d_queries: bfloat16 [16384, 8192], P('seg', 'exp')
- d_keys: bfloat16 [16384, 8192], P('seg', 'exp')
- d_values: bfloat16 [16384, 8192], P('seg', 'exp')
The draws below stay inside these ranges and needn't reach their ends.
All inputs are finite; a program needn't handle non-finite values.
Results may differ from the reference program's by a relative error of at most 0.0063.
Values sent between devices are 32-bit elements; how exact they have to be, the bound alone decides.
No kernel may reach another device: no remote copies, remote signals or barrier semaphores. Data moves between devices by JAX's collectives and lax.ppermute only.
A program may use at most 64 MiB of HBM per device.

```python
import jax
import jax.numpy as jnp
from jax import lax

E = 128
HEADS = 64
FEAT = 8192
SEQ = 16384
BLK = 512


def draw_log_decay(key, part):
    keys_list = jax.random.split(key, 6)
    share = 0.5
    fast = jax.random.uniform(keys_list[0], (HEADS, 1)) < share
    quick = jnp.exp(jax.random.uniform(keys_list[1], (HEADS, 1), minval=jnp.log(1.0 / 50.0), maxval=jnp.log(1.0 / 30.0)))
    slow = jnp.exp(jax.random.uniform(keys_list[2], (HEADS, 1), minval=jnp.log(0.05), maxval=0.0)) / SEQ
    decay_rate = jnp.where(fast, quick, slow)
    approximate_output = jax.random.uniform(keys_list[3], (HEADS, SEQ), minval=0.5, maxval=1.5)
    place_indices = jax.random.randint(keys_list[4], (HEADS, 2), 0, SEQ)
    retained_factor = jax.random.uniform(keys_list[5], (HEADS, 2), minval=0.6, maxval=0.8)
    token_place = jnp.arange(SEQ)
    token_group = jnp.sum(jnp.where(token_place[None, :, None] == place_indices[:, None, :], jnp.log(retained_factor)[:, None, :], 0.0), axis=-1)
    return (token_group - decay_rate * approximate_output).astype(jnp.float32)


def draw_values(key, part):
    keys_list = jax.random.split(key, 2)
    level = jnp.arange(HEADS).astype(jnp.float32) / (HEADS - 1)
    noise = jnp.clip(jax.random.normal(keys_list[0], (SEQ, FEAT)), -5.0, 5.0)
    rows_level = jax.random.uniform(keys_list[1], (SEQ, 1), minval=0.0, maxval=1.0)
    columns = jnp.repeat(10.0 ** level, E)
    return (noise * 10.0 ** rows_level * columns[None, :]).astype(jnp.bfloat16)


def shard_levels(own_key, extent, cuts, least, top_value):
    def one(dim, blocks):
        draws = jax.random.uniform(jax.random.fold_in(jax.random.fold_in(own_key, 6), dim), (blocks,), jnp.float32, least / len(cuts), top_value / len(cuts))
        return jnp.repeat(jnp.exp(draws), extent[dim] // blocks).reshape((-1,) + (1,) * (len(extent) - dim - 1))

    loudness = one(*cuts[0])
    for cut in cuts[1:]:
        loudness = loudness * one(*cut)
    return loudness


def gaussian(own_key, dims, scale, limit, cuts=(), dtype=jnp.bfloat16):
    result = scale * jax.random.normal(own_key, dims, jnp.float32)
    if cuts:
        result = result * shard_levels(own_key, dims, cuts, -0.22, 0.18)
    return jnp.clip(result, -limit, limit).astype(dtype)


def setup_inputs(seed: int = 0) -> dict:
    seeds = jax.random.split(jax.random.key(seed), 7)
    queries = gaussian(seeds[0], (SEQ, FEAT), 1.0, 6.0, ((0, 16), (1, 32)))
    keys = gaussian(seeds[1], (SEQ, FEAT), (E ** -0.5), 0.52734375, ((0, 16), (1, 32)))
    values = draw_values(jax.random.fold_in(seeds[6], 71), 0)
    log_decay = draw_log_decay(jax.random.fold_in(seeds[6], 71), 0)
    gain = jnp.clip(1.0 + 0.1 * jax.random.normal(seeds[4], (FEAT,), jnp.float32), 0.5, 1.5)
    d_out = gaussian(seeds[5], (SEQ, FEAT), 1.0, 6.0, ((0, 16), (1, 32)))
    return dict(queries=queries, keys=keys, values=values, log_decay=log_decay, gain=gain, d_out=d_out)


EPS = 1e-06

def decay_parts(log_block):
    cumulative = jnp.cumsum(log_block, axis=-1)
    length = log_block.shape[-1]
    spread = cumulative[..., :, None] - cumulative[..., None, :]
    token_place = jnp.arange(length)
    lower = token_place[:, None] >= token_place[None, :]
    mask = jnp.where(lower, jnp.exp(jnp.minimum(spread, 0.0)), 0.0)
    return (cumulative, cumulative[..., -1], mask)

def rounded(value):
    return lax.optimization_barrier(value.astype(jnp.bfloat16)).astype(jnp.float32)

def reference(queries, keys, values, log_decay, gain, d_out):
    count = SEQ // BLK
    qsteps = queries.reshape(count, BLK, HEADS, E)
    ksteps = keys.reshape(count, BLK, HEADS, E)
    vsteps = values.reshape(count, BLK, HEADS, E)
    lower_step_count = log_decay.reshape(HEADS, count, BLK).transpose(1, 0, 2)

    def forward(state, inputs):
        qblock, kblock, vblock, lblock = inputs
        cumulative, totals, mask = decay_parts(lblock)
        qf = qblock.astype(jnp.float32)
        kf = kblock.astype(jnp.float32)
        vf = vblock.astype(jnp.float32)
        scores = rounded(jnp.einsum('the,she->hts', qf, kf) * mask)
        inner = jnp.einsum('hts,shf->thf', scores, vf)
        held = rounded(state)
        grow = jnp.exp(cumulative).T[:, :, None]
        outer = jnp.einsum('the,hef->thf', qf, held) * grow
        shrink = jnp.exp(totals[:, None] - cumulative).T[:, :, None]
        key_weighted = rounded(kf * shrink)
        state = jnp.exp(totals)[:, None, None] * state + jnp.einsum('she,shf->hef', key_weighted, vf)
        return (state, (inner + outer, held))
    zero = jnp.zeros((HEADS, E, E), jnp.float32)
    _, (attended, helds) = lax.scan(forward, zero, (qsteps, ksteps, vsteps, lower_step_count))
    attended = attended.reshape(SEQ, FEAT)
    upstream = d_out.astype(jnp.float32)
    squares = lax.optimization_barrier(jnp.sum(attended * attended, axis=-1))
    cross = lax.optimization_barrier(jnp.sum(gain * upstream * attended, axis=-1))
    inv_rms = lax.rsqrt(squares / FEAT + EPS)[:, None]
    out = (attended * inv_rms * gain).astype(jnp.bfloat16)
    grad_attended = (gain * upstream * inv_rms - attended * inv_rms * inv_rms * inv_rms * cross[:, None] / FEAT).astype(jnp.bfloat16)
    gsteps = grad_attended.reshape(count, BLK, HEADS, E)

    def backward(carry, inputs):
        qblock, kblock, vblock, lblock, gblock, held = inputs
        cumulative, totals, mask = decay_parts(lblock)
        qf = qblock.astype(jnp.float32)
        kf = kblock.astype(jnp.float32)
        vf = vblock.astype(jnp.float32)
        gf = gblock.astype(jnp.float32)
        scores = rounded(jnp.einsum('the,she->hts', qf, kf) * mask)
        grad_scores = rounded(jnp.einsum('thf,shf->hts', gf, vf) * mask)
        exits = rounded(carry)
        grow = jnp.exp(cumulative).T[:, :, None]
        shrink = jnp.exp(totals[:, None] - cumulative).T[:, :, None]
        grad_q = jnp.einsum('hts,she->the', grad_scores, kf) + grow * jnp.einsum('thf,hef->the', gf, held)
        grad_k = jnp.einsum('hts,the->she', grad_scores, qf) + shrink * jnp.einsum('shf,hef->she', vf, exits)
        grad_v = jnp.einsum('hts,thf->shf', scores, gf) + shrink * jnp.einsum('she,hef->shf', kf, exits)
        query_weighted = rounded(qf * grow)
        carry = jnp.exp(totals)[:, None, None] * carry + jnp.einsum('the,thf->hef', query_weighted, gf)
        return (carry, (grad_q.astype(jnp.bfloat16), grad_k.astype(jnp.bfloat16), grad_v.astype(jnp.bfloat16)))
    _, (grad_q, grad_k, grad_v) = lax.scan(backward, zero, (qsteps, ksteps, vsteps, lower_step_count, gsteps, helds), reverse=True)
    return (out, grad_q.reshape(SEQ, FEAT), grad_k.reshape(SEQ, FEAT), grad_v.reshape(SEQ, FEAT))
```

```python
import jax
import jax.numpy as jnp
from jax import lax
from jax.sharding import PartitionSpec as P

BLK = 512


EPS = 1e-06


def decay_parts(log_block):
    cumulative = jnp.cumsum(log_block, axis=-1)
    length = log_block.shape[-1]
    spread = cumulative[..., :, None] - cumulative[..., None, :]
    token_place = jnp.arange(length)
    lower = token_place[:, None] >= token_place[None, :]
    mask = jnp.where(lower, jnp.exp(jnp.minimum(spread, 0.0)), 0.0)
    return (cumulative, cumulative[..., -1], mask)


def body(queries, keys, values, log_decay, gain, d_out):
    rows, width = queries.shape
    local_heads = log_decay.shape[0]
    head_width = width // local_heads
    count = rows // BLK
    shape = (count, BLK, local_heads, head_width)
    qblocks = queries.reshape(shape)
    kblocks = keys.reshape(shape)
    vblocks = values.reshape(shape)
    lblocks = log_decay.reshape(local_heads, count, BLK).transpose(1, 0, 2)
    cumulative, totals, mask = decay_parts(lblocks)
    grow = jnp.exp(cumulative).transpose(0, 2, 1)[..., None]
    shrink = jnp.exp(totals[:, None, :] - cumulative.transpose(0, 2, 1))[..., None]
    scores = (
        jnp.einsum("bthe,bshe->bhts", qblocks, kblocks, preferred_element_type=jnp.float32) * mask
    ).astype(jnp.bfloat16)
    inner = jnp.einsum("bhts,bshf->bthf", scores, vblocks, preferred_element_type=jnp.float32)
    key_weighted = (kblocks * shrink).astype(jnp.bfloat16)
    block_state = jnp.einsum(
        "bshe,bshf->bhef", key_weighted, vblocks, preferred_element_type=jnp.float32
    )
    block_fade = jnp.exp(totals)
    seg_count = lax.axis_size("seg")
    here = lax.axis_index("seg")
    seg_state = block_state[0]
    for block in range(1, count):
        seg_state = block_fade[block][:, None, None] * seg_state + block_state[block]
    seg_log = jnp.sum(log_decay, axis=-1)
    log_rows = jnp.broadcast_to(seg_log[:, None, None], (local_heads, 8, head_width))
    gathered = lax.all_gather(jnp.concatenate((seg_state, log_rows), axis=1), "seg")
    all_states = gathered[:, :, :head_width, :]
    all_logs = gathered[:, :, head_width, 0]
    places = jnp.arange(seg_count)
    between_fwd = (places[:, None] < places[None, :]) & (places[None, :] < here)
    between_bwd = (places[:, None] > places[None, :]) & (places[None, :] > here)
    weight_fwd = jnp.where(
        (places < here)[:, None],
        jnp.exp(jnp.sum(jnp.where(between_fwd[:, :, None], all_logs[None, :, :], 0.0), axis=1)),
        0.0,
    )
    weight_bwd = jnp.where(
        (places > here)[:, None],
        jnp.exp(jnp.sum(jnp.where(between_bwd[:, :, None], all_logs[None, :, :], 0.0), axis=1)),
        0.0,
    )
    entering = jnp.sum(weight_fwd[:, :, None, None] * all_states, axis=0)
    held_list = []
    running = entering
    for block in range(count):
        held_list.append(running.astype(jnp.bfloat16))
        running = block_fade[block][:, None, None] * running + block_state[block]
    held = jnp.stack(held_list)
    attended = inner + grow * jnp.einsum(
        "bthe,bhef->bthf", qblocks, held, preferred_element_type=jnp.float32
    )
    attended = attended.reshape(rows, width)
    upstream = d_out.astype(jnp.float32)
    partial = jnp.stack(
        (jnp.sum(attended * attended, axis=-1), jnp.sum(gain * upstream * attended, axis=-1))
    )
    totals_exp = jnp.sum(lax.all_gather(jnp.concatenate((partial, jnp.zeros((6, partial.shape[1]), partial.dtype))), "exp"), axis=0)[:2]
    squares, cross = totals_exp[0], totals_exp[1]
    features = width * lax.axis_size("exp")
    inv_rms = lax.rsqrt(squares / features + EPS)[:, None]
    out = (attended * inv_rms * gain).astype(jnp.bfloat16)
    grad_attended = (
        gain * upstream * inv_rms
        - attended * inv_rms * inv_rms * inv_rms * cross[:, None] / features
    ).astype(jnp.bfloat16)
    grad_blocks = grad_attended.reshape(shape)
    query_weighted = (qblocks * grow).astype(jnp.bfloat16)
    back_terms = jnp.einsum(
        "bthe,bthf->bhef", query_weighted, grad_blocks, preferred_element_type=jnp.float32
    )
    seg_back = back_terms[count - 1]
    for block in range(count - 2, -1, -1):
        seg_back = back_terms[block] + block_fade[block][:, None, None] * seg_back
    all_backs = lax.all_gather(seg_back, "seg")
    leaving = jnp.sum(weight_bwd[:, :, None, None] * all_backs, axis=0)
    exit_list = [None] * count
    running = leaving
    for block in range(count - 1, -1, -1):
        exit_list[block] = running.astype(jnp.bfloat16)
        running = back_terms[block] + block_fade[block][:, None, None] * running
    exits = jnp.stack(exit_list)
    grad_scores = (
        jnp.einsum("bthf,bshf->bhts", grad_blocks, vblocks, preferred_element_type=jnp.float32)
        * mask
    ).astype(jnp.bfloat16)
    grad_q = jnp.einsum("bhts,bshe->bthe", grad_scores, kblocks, preferred_element_type=jnp.float32)
    grad_q = grad_q + grow * jnp.einsum(
        "bthf,bhef->bthe", grad_blocks, held, preferred_element_type=jnp.float32
    )
    grad_k = jnp.einsum("bhts,bthe->bshe", grad_scores, qblocks, preferred_element_type=jnp.float32)
    grad_k = grad_k + shrink * jnp.einsum(
        "bshf,bhef->bshe", vblocks, exits, preferred_element_type=jnp.float32
    )
    grad_v = jnp.einsum("bhts,bthf->bshf", scores, grad_blocks, preferred_element_type=jnp.float32)
    grad_v = grad_v + shrink * jnp.einsum(
        "bshe,bhef->bshf", kblocks, exits, preferred_element_type=jnp.float32
    )
    return (
        out,
        grad_q.reshape(rows, width).astype(jnp.bfloat16),
        grad_k.reshape(rows, width).astype(jnp.bfloat16),
        grad_v.reshape(rows, width).astype(jnp.bfloat16),
    )


def solution(mesh):
    in_specs = (
        P("seg", "exp"),
        P("seg", "exp"),
        P("seg", "exp"),
        P("exp", "seg"),
        P("exp"),
        P("seg", "exp"),
    )
    out_specs = (P("seg", "exp"), P("seg", "exp"), P("seg", "exp"), P("seg", "exp"))
    return jax.shard_map(body, mesh=mesh, in_specs=in_specs, out_specs=out_specs, check_vma=False)
```

```python
import jax
import jax.numpy as jnp
from jax import lax
from jax.sharding import PartitionSpec as P

BLK = 512
EXP_PARTS = ("exp_y", "exp_x", "exp_core")


EPS = 1e-06


def decay_parts(log_block):
    cumulative = jnp.cumsum(log_block, axis=-1)
    length = log_block.shape[-1]
    spread = cumulative[..., :, None] - cumulative[..., None, :]
    token_place = jnp.arange(length)
    lower = token_place[:, None] >= token_place[None, :]
    mask = jnp.where(lower, jnp.exp(jnp.minimum(spread, 0.0)), 0.0)
    return (cumulative, cumulative[..., -1], mask)


def body(queries, keys, values, log_decay, gain, d_out):
    rows, width = queries.shape
    local_heads = log_decay.shape[0]
    head_width = width // local_heads
    count = rows // BLK
    shape = (count, BLK, local_heads, head_width)
    qblocks = queries.reshape(shape)
    kblocks = keys.reshape(shape)
    vblocks = values.reshape(shape)
    lblocks = log_decay.reshape(local_heads, count, BLK).transpose(1, 0, 2)
    cumulative, totals, mask = decay_parts(lblocks)
    grow = jnp.exp(cumulative).transpose(0, 2, 1)[..., None]
    shrink = jnp.exp(totals[:, None, :] - cumulative.transpose(0, 2, 1))[..., None]
    scores = (
        jnp.einsum("bthe,bshe->bhts", qblocks, kblocks, preferred_element_type=jnp.float32) * mask
    ).astype(jnp.bfloat16)
    inner = jnp.einsum("bhts,bshf->bthf", scores, vblocks, preferred_element_type=jnp.float32)
    key_weighted = (kblocks * shrink).astype(jnp.bfloat16)
    block_state = jnp.einsum(
        "bshe,bshf->bhef", key_weighted, vblocks, preferred_element_type=jnp.float32
    )
    block_fade = jnp.exp(totals)
    seg_count = lax.axis_size("seg")
    here = lax.axis_index("seg")
    seg_state = block_state[0]
    for block in range(1, count):
        seg_state = block_fade[block][:, None, None] * seg_state + block_state[block]
    seg_log = jnp.sum(log_decay, axis=-1)
    log_rows = jnp.broadcast_to(seg_log[:, None, None], (local_heads, 8, head_width))
    gathered = lax.all_gather(jnp.concatenate((seg_state, log_rows), axis=1), "seg")
    all_states = gathered[:, :, :head_width, :]
    all_logs = gathered[:, :, head_width, 0]
    places = jnp.arange(seg_count)
    between_fwd = (places[:, None] < places[None, :]) & (places[None, :] < here)
    between_bwd = (places[:, None] > places[None, :]) & (places[None, :] > here)
    weight_fwd = jnp.where(
        (places < here)[:, None],
        jnp.exp(jnp.sum(jnp.where(between_fwd[:, :, None], all_logs[None, :, :], 0.0), axis=1)),
        0.0,
    )
    weight_bwd = jnp.where(
        (places > here)[:, None],
        jnp.exp(jnp.sum(jnp.where(between_bwd[:, :, None], all_logs[None, :, :], 0.0), axis=1)),
        0.0,
    )
    entering = jnp.sum(weight_fwd[:, :, None, None] * all_states, axis=0)
    held_list = []
    running = entering
    for block in range(count):
        held_list.append(running.astype(jnp.bfloat16))
        running = block_fade[block][:, None, None] * running + block_state[block]
    held = jnp.stack(held_list)
    attended = inner + grow * jnp.einsum(
        "bthe,bhef->bthf", qblocks, held, preferred_element_type=jnp.float32
    )
    attended = attended.reshape(rows, width)
    upstream = d_out.astype(jnp.float32)
    partial = jnp.stack(
        (jnp.sum(attended * attended, axis=-1), jnp.sum(gain * upstream * attended, axis=-1))
    )
    totals_exp = partial
    for axis in EXP_PARTS[::-1]:
        totals_exp = lax.psum(totals_exp, axis)
    squares, cross = totals_exp[0], totals_exp[1]
    features = width * lax.axis_size(EXP_PARTS)
    inv_rms = lax.rsqrt(squares / features + EPS)[:, None]
    out = (attended * inv_rms * gain).astype(jnp.bfloat16)
    grad_attended = (
        gain * upstream * inv_rms
        - attended * inv_rms * inv_rms * inv_rms * cross[:, None] / features
    ).astype(jnp.bfloat16)
    grad_blocks = grad_attended.reshape(shape)
    query_weighted = (qblocks * grow).astype(jnp.bfloat16)
    back_terms = jnp.einsum(
        "bthe,bthf->bhef", query_weighted, grad_blocks, preferred_element_type=jnp.float32
    )
    seg_back = back_terms[count - 1]
    for block in range(count - 2, -1, -1):
        seg_back = back_terms[block] + block_fade[block][:, None, None] * seg_back
    all_backs = lax.all_gather(seg_back, "seg")
    leaving = jnp.sum(weight_bwd[:, :, None, None] * all_backs, axis=0)
    exit_list = [None] * count
    running = leaving
    for block in range(count - 1, -1, -1):
        exit_list[block] = running.astype(jnp.bfloat16)
        running = back_terms[block] + block_fade[block][:, None, None] * running
    exits = jnp.stack(exit_list)
    grad_scores = (
        jnp.einsum("bthf,bshf->bhts", grad_blocks, vblocks, preferred_element_type=jnp.float32)
        * mask
    ).astype(jnp.bfloat16)
    grad_q = jnp.einsum("bhts,bshe->bthe", grad_scores, kblocks, preferred_element_type=jnp.float32)
    grad_q = grad_q + grow * jnp.einsum(
        "bthf,bhef->bthe", grad_blocks, held, preferred_element_type=jnp.float32
    )
    grad_k = jnp.einsum("bhts,bthe->bshe", grad_scores, qblocks, preferred_element_type=jnp.float32)
    grad_k = grad_k + shrink * jnp.einsum(
        "bshf,bhef->bshe", vblocks, exits, preferred_element_type=jnp.float32
    )
    grad_v = jnp.einsum("bhts,bthf->bshf", scores, grad_blocks, preferred_element_type=jnp.float32)
    grad_v = grad_v + shrink * jnp.einsum(
        "bshe,bhef->bshf", kblocks, exits, preferred_element_type=jnp.float32
    )
    return (
        out,
        grad_q.reshape(rows, width).astype(jnp.bfloat16),
        grad_k.reshape(rows, width).astype(jnp.bfloat16),
        grad_v.reshape(rows, width).astype(jnp.bfloat16),
    )


def solution(mesh):
    parts = mesh.devices.reshape(mesh.devices.shape[0], 4, -1, 2)
    split = jax.sharding.Mesh(parts, ("seg",) + EXP_PARTS)
    rows_heads = P("seg", EXP_PARTS)
    in_specs = (rows_heads, rows_heads, rows_heads, P(EXP_PARTS, "seg"), P(EXP_PARTS), rows_heads)
    out_specs = (rows_heads, rows_heads, rows_heads, rows_heads)
    return jax.shard_map(body, mesh=split, in_specs=in_specs, out_specs=out_specs, check_vma=False)
```

```python
import jax
import jax.numpy as jnp
from jax import lax
from jax.sharding import PartitionSpec as P

BLK = 512
EXP_PARTS = ("exp_y", "exp_x", "exp_core")
SEG_PARTS = ("seg_hi", "seg_lo")


EPS = 1e-06


def decay_parts(log_block):
    cumulative = jnp.cumsum(log_block, axis=-1)
    length = log_block.shape[-1]
    spread = cumulative[..., :, None] - cumulative[..., None, :]
    token_place = jnp.arange(length)
    lower = token_place[:, None] >= token_place[None, :]
    mask = jnp.where(lower, jnp.exp(jnp.minimum(spread, 0.0)), 0.0)
    return (cumulative, cumulative[..., -1], mask)


def fade_weights(order, valid, logs, limit, extra=0.0):
    between = order & limit
    summed = jnp.sum(jnp.where(between[:, :, None], logs[None, :, :], 0.0), axis=1) + extra
    return jnp.where(valid[:, None], jnp.exp(summed), 0.0)


def body(queries, keys, values, log_decay, gain, d_out):
    rows, width = queries.shape
    local_heads = log_decay.shape[0]
    head_width = width // local_heads
    count = rows // BLK
    shape = (count, BLK, local_heads, head_width)
    qblocks = queries.reshape(shape)
    kblocks = keys.reshape(shape)
    vblocks = values.reshape(shape)
    lblocks = log_decay.reshape(local_heads, count, BLK).transpose(1, 0, 2)
    cumulative, totals, mask = decay_parts(lblocks)
    grow = jnp.exp(cumulative).transpose(0, 2, 1)[..., None]
    shrink = jnp.exp(totals[:, None, :] - cumulative.transpose(0, 2, 1))[..., None]
    scores = (
        jnp.einsum("bthe,bshe->bhts", qblocks, kblocks, preferred_element_type=jnp.float32) * mask
    ).astype(jnp.bfloat16)
    inner = jnp.einsum("bhts,bshf->bthf", scores, vblocks, preferred_element_type=jnp.float32)
    key_weighted = (kblocks * shrink).astype(jnp.bfloat16)
    block_state = jnp.einsum(
        "bshe,bshf->bhef", key_weighted, vblocks, preferred_element_type=jnp.float32
    )
    block_fade = jnp.exp(totals)
    seg_state = block_state[0]
    for block in range(1, count):
        seg_state = block_fade[block][:, None, None] * seg_state + block_state[block]
    low = lax.axis_index("seg_lo")
    high = lax.axis_index("seg_hi")
    low_places = jnp.arange(lax.axis_size("seg_lo"))
    high_places = jnp.arange(lax.axis_size("seg_hi"))
    seg_log = jnp.sum(log_decay, axis=-1)
    log_rows = jnp.broadcast_to(seg_log[:, None, None], (local_heads, 8, head_width))
    first = lax.all_gather(jnp.concatenate((seg_state, log_rows), axis=1), "seg_lo")
    low_states = first[:, :, :head_width, :]
    low_logs = first[:, :, head_width, 0]
    inside = fade_weights(low_places[:, None] < low_places[None, :], low_places < low, low_logs, low_places[None, :] < low)
    within = jnp.sum(inside[:, :, None, None] * low_states, axis=0)
    to_end = fade_weights(low_places[:, None] < low_places[None, :], low_places >= 0, low_logs, True)
    group_state = jnp.sum(to_end[:, :, None, None] * low_states, axis=0)
    group_log = jnp.sum(low_logs, axis=0)
    group_rows = jnp.broadcast_to(group_log[:, None, None], (local_heads, 8, head_width))
    second = lax.all_gather(jnp.concatenate((group_state, group_rows), axis=1), "seg_hi")
    high_states = second[:, :, :head_width, :]
    high_logs = second[:, :, head_width, 0]
    before_here = jnp.sum(jnp.where((low_places < low)[:, None], low_logs, 0.0), axis=0)
    outside = fade_weights(
        high_places[:, None] < high_places[None, :], high_places < high, high_logs, high_places[None, :] < high, before_here
    )
    entering = within + jnp.sum(outside[:, :, None, None] * high_states, axis=0)
    held_list = []
    running = entering
    for block in range(count):
        held_list.append(running.astype(jnp.bfloat16))
        running = block_fade[block][:, None, None] * running + block_state[block]
    held = jnp.stack(held_list)
    attended = inner + grow * jnp.einsum(
        "bthe,bhef->bthf", qblocks, held, preferred_element_type=jnp.float32
    )
    attended = attended.reshape(rows, width)
    upstream = d_out.astype(jnp.float32)
    partial = jnp.stack(
        (jnp.sum(attended * attended, axis=-1), jnp.sum(gain * upstream * attended, axis=-1))
    )
    totals_exp = partial
    for axis in EXP_PARTS[::-1]:
        totals_exp = lax.psum(totals_exp, axis)
    squares, cross = totals_exp[0], totals_exp[1]
    features = width * lax.axis_size(EXP_PARTS)
    inv_rms = lax.rsqrt(squares / features + EPS)[:, None]
    out = (attended * inv_rms * gain).astype(jnp.bfloat16)
    grad_attended = (
        gain * upstream * inv_rms
        - attended * inv_rms * inv_rms * inv_rms * cross[:, None] / features
    ).astype(jnp.bfloat16)
    grad_blocks = grad_attended.reshape(shape)
    query_weighted = (qblocks * grow).astype(jnp.bfloat16)
    back_terms = jnp.einsum(
        "bthe,bthf->bhef", query_weighted, grad_blocks, preferred_element_type=jnp.float32
    )
    seg_back = back_terms[count - 1]
    for block in range(count - 2, -1, -1):
        seg_back = back_terms[block] + block_fade[block][:, None, None] * seg_back
    third = lax.all_gather(seg_back, "seg_lo")
    inside_back = fade_weights(low_places[:, None] > low_places[None, :], low_places > low, low_logs, low_places[None, :] > low)
    within_back = jnp.sum(inside_back[:, :, None, None] * third, axis=0)
    to_start = fade_weights(low_places[:, None] > low_places[None, :], low_places >= 0, low_logs, True)
    group_back = jnp.sum(to_start[:, :, None, None] * third, axis=0)
    fourth = lax.all_gather(group_back, "seg_hi")
    after_here = jnp.sum(jnp.where((low_places > low)[:, None], low_logs, 0.0), axis=0)
    outside_back = fade_weights(
        high_places[:, None] > high_places[None, :], high_places > high, high_logs, high_places[None, :] > high, after_here
    )
    leaving = within_back + jnp.sum(outside_back[:, :, None, None] * fourth, axis=0)
    exit_list = [None] * count
    running = leaving
    for block in range(count - 1, -1, -1):
        exit_list[block] = running.astype(jnp.bfloat16)
        running = back_terms[block] + block_fade[block][:, None, None] * running
    exits = jnp.stack(exit_list)
    grad_scores = (
        jnp.einsum("bthf,bshf->bhts", grad_blocks, vblocks, preferred_element_type=jnp.float32)
        * mask
    ).astype(jnp.bfloat16)
    grad_q = jnp.einsum("bhts,bshe->bthe", grad_scores, kblocks, preferred_element_type=jnp.float32)
    grad_q = grad_q + grow * jnp.einsum(
        "bthf,bhef->bthe", grad_blocks, held, preferred_element_type=jnp.float32
    )
    grad_k = jnp.einsum("bhts,bthe->bshe", grad_scores, qblocks, preferred_element_type=jnp.float32)
    grad_k = grad_k + shrink * jnp.einsum(
        "bshf,bhef->bshe", vblocks, exits, preferred_element_type=jnp.float32
    )
    grad_v = jnp.einsum("bhts,bthf->bshf", scores, grad_blocks, preferred_element_type=jnp.float32)
    grad_v = grad_v + shrink * jnp.einsum(
        "bshe,bhef->bshf", kblocks, exits, preferred_element_type=jnp.float32
    )
    return (
        out,
        grad_q.reshape(rows, width).astype(jnp.bfloat16),
        grad_k.reshape(rows, width).astype(jnp.bfloat16),
        grad_v.reshape(rows, width).astype(jnp.bfloat16),
    )


def solution(mesh):
    parts = mesh.devices.reshape(4, -1, 4, mesh.devices.shape[1] // 8, 2)
    split = jax.sharding.Mesh(parts, SEG_PARTS + EXP_PARTS)
    rows_heads = P(SEG_PARTS, EXP_PARTS)
    in_specs = (rows_heads, rows_heads, rows_heads, P(EXP_PARTS, SEG_PARTS), P(EXP_PARTS), rows_heads)
    out_specs = (rows_heads, rows_heads, rows_heads, rows_heads)
    return jax.shard_map(body, mesh=split, in_specs=in_specs, out_specs=out_specs, check_vma=False)
```

```python
import jax
import jax.numpy as jnp
from jax import lax
from jax.sharding import PartitionSpec as P

BLK = 512
EXP_PARTS = ("exp_y", "exp_x", "exp_core")
SEG_PARTS = ("seg_hi", "seg_lo")


EPS = 1e-06


def decay_parts(log_block):
    cumulative = jnp.cumsum(log_block, axis=-1)
    length = log_block.shape[-1]
    spread = cumulative[..., :, None] - cumulative[..., None, :]
    token_place = jnp.arange(length)
    lower = token_place[:, None] >= token_place[None, :]
    mask = jnp.where(lower, jnp.exp(jnp.minimum(spread, 0.0)), 0.0)
    return (cumulative, cumulative[..., -1], mask)


def fade_weights(order, valid, logs, limit, extra=0.0):
    between = order & limit
    summed = jnp.sum(jnp.where(between[:, :, None], logs[None, :, :], 0.0), axis=1) + extra
    return jnp.where(valid[:, None], jnp.exp(summed), 0.0)


def body(queries, keys, values, log_decay, gain, d_out):
    rows, width = queries.shape
    local_heads = log_decay.shape[0]
    head_width = width // local_heads
    count = rows // BLK
    shape = (count, BLK, local_heads, head_width)
    qblocks = queries.reshape(shape)
    kblocks = keys.reshape(shape)
    vblocks = values.reshape(shape)
    lblocks = log_decay.reshape(local_heads, count, BLK).transpose(1, 0, 2)
    cumulative, totals, mask = decay_parts(lblocks)
    grow = jnp.exp(cumulative).transpose(0, 2, 1)[..., None]
    shrink = jnp.exp(totals[:, None, :] - cumulative.transpose(0, 2, 1))[..., None]
    scores = (
        jnp.einsum("bthe,bshe->bhts", qblocks, kblocks, preferred_element_type=jnp.float32) * mask
    ).astype(jnp.bfloat16)
    inner = jnp.einsum("bhts,bshf->bthf", scores, vblocks, preferred_element_type=jnp.float32)
    key_weighted = (kblocks * shrink).astype(jnp.bfloat16)
    block_state = jnp.einsum(
        "bshe,bshf->bhef", key_weighted, vblocks, preferred_element_type=jnp.float32
    )
    block_fade = jnp.exp(totals)
    seg_state = block_state[0]
    for block in range(1, count):
        seg_state = block_fade[block][:, None, None] * seg_state + block_state[block]
    low = lax.axis_index("seg_lo")
    high = lax.axis_index("seg_hi")
    low_places = jnp.arange(lax.axis_size("seg_lo"))
    high_places = jnp.arange(lax.axis_size("seg_hi"))
    seg_log = jnp.sum(log_decay, axis=-1)
    log_rows = jnp.broadcast_to(seg_log[:, None, None], (local_heads, 8, head_width))
    first = lax.all_gather(jnp.concatenate((seg_state, log_rows), axis=1), "seg_lo")
    low_states = first[:, :, :head_width, :]
    low_logs = first[:, :, head_width, 0]
    inside = fade_weights(low_places[:, None] < low_places[None, :], low_places < low, low_logs, low_places[None, :] < low)
    within = jnp.sum(inside[:, :, None, None] * low_states, axis=0)
    to_end = fade_weights(low_places[:, None] < low_places[None, :], low_places >= 0, low_logs, True)
    group_state = jnp.sum(to_end[:, :, None, None] * low_states, axis=0)
    group_log = jnp.sum(low_logs, axis=0)
    group_rows = jnp.broadcast_to(group_log[:, None, None], (local_heads, 8, head_width))
    second = lax.all_gather(jnp.concatenate((group_state, group_rows), axis=1), "seg_hi")
    high_states = second[:, :, :head_width, :]
    high_logs = second[:, :, head_width, 0]
    before_here = jnp.sum(jnp.where((low_places < low)[:, None], low_logs, 0.0), axis=0)
    outside = fade_weights(
        high_places[:, None] < high_places[None, :], high_places < high, high_logs, high_places[None, :] < high, before_here
    )
    entering = within + jnp.sum(outside[:, :, None, None] * high_states, axis=0)
    held_list = []
    running = entering
    for block in range(count):
        held_list.append(running.astype(jnp.bfloat16))
        running = block_fade[block][:, None, None] * running + block_state[block]
    held = jnp.stack(held_list)
    attended = inner + grow * jnp.einsum(
        "bthe,bhef->bthf", qblocks, held, preferred_element_type=jnp.float32
    )
    attended = attended.reshape(rows, width)
    upstream = d_out.astype(jnp.float32)
    partial = jnp.stack(
        (jnp.sum(attended * attended, axis=-1), jnp.sum(gain * upstream * attended, axis=-1))
    )
    totals_exp = lax.psum(partial, EXP_PARTS[-1])
    for axis in EXP_PARTS[-2::-1]:
        totals_exp = jnp.sum(lax.all_gather(totals_exp, axis), axis=0)
    squares, cross = totals_exp[0], totals_exp[1]
    features = width * lax.axis_size(EXP_PARTS)
    inv_rms = lax.rsqrt(squares / features + EPS)[:, None]
    out = (attended * inv_rms * gain).astype(jnp.bfloat16)
    grad_attended = (
        gain * upstream * inv_rms
        - attended * inv_rms * inv_rms * inv_rms * cross[:, None] / features
    ).astype(jnp.bfloat16)
    grad_blocks = grad_attended.reshape(shape)
    query_weighted = (qblocks * grow).astype(jnp.bfloat16)
    back_terms = jnp.einsum(
        "bthe,bthf->bhef", query_weighted, grad_blocks, preferred_element_type=jnp.float32
    )
    seg_back = back_terms[count - 1]
    for block in range(count - 2, -1, -1):
        seg_back = back_terms[block] + block_fade[block][:, None, None] * seg_back
    third = lax.all_gather(seg_back, "seg_lo")
    inside_back = fade_weights(low_places[:, None] > low_places[None, :], low_places > low, low_logs, low_places[None, :] > low)
    within_back = jnp.sum(inside_back[:, :, None, None] * third, axis=0)
    to_start = fade_weights(low_places[:, None] > low_places[None, :], low_places >= 0, low_logs, True)
    group_back = jnp.sum(to_start[:, :, None, None] * third, axis=0)
    fourth = lax.all_gather(group_back, "seg_hi")
    after_here = jnp.sum(jnp.where((low_places > low)[:, None], low_logs, 0.0), axis=0)
    outside_back = fade_weights(
        high_places[:, None] > high_places[None, :], high_places > high, high_logs, high_places[None, :] > high, after_here
    )
    leaving = within_back + jnp.sum(outside_back[:, :, None, None] * fourth, axis=0)
    exit_list = [None] * count
    running = leaving
    for block in range(count - 1, -1, -1):
        exit_list[block] = running.astype(jnp.bfloat16)
        running = back_terms[block] + block_fade[block][:, None, None] * running
    exits = jnp.stack(exit_list)
    grad_scores = (
        jnp.einsum("bthf,bshf->bhts", grad_blocks, vblocks, preferred_element_type=jnp.float32)
        * mask
    ).astype(jnp.bfloat16)
    grad_q = jnp.einsum("bhts,bshe->bthe", grad_scores, kblocks, preferred_element_type=jnp.float32)
    grad_q = grad_q + grow * jnp.einsum(
        "bthf,bhef->bthe", grad_blocks, held, preferred_element_type=jnp.float32
    )
    grad_k = jnp.einsum("bhts,bthe->bshe", grad_scores, qblocks, preferred_element_type=jnp.float32)
    grad_k = grad_k + shrink * jnp.einsum(
        "bshf,bhef->bshe", vblocks, exits, preferred_element_type=jnp.float32
    )
    grad_v = jnp.einsum("bhts,bthf->bshf", scores, grad_blocks, preferred_element_type=jnp.float32)
    grad_v = grad_v + shrink * jnp.einsum(
        "bshe,bhef->bshf", kblocks, exits, preferred_element_type=jnp.float32
    )
    return (
        out,
        grad_q.reshape(rows, width).astype(jnp.bfloat16),
        grad_k.reshape(rows, width).astype(jnp.bfloat16),
        grad_v.reshape(rows, width).astype(jnp.bfloat16),
    )


def solution(mesh):
    parts = mesh.devices.reshape(4, -1, 4, mesh.devices.shape[1] // 8, 2)
    split = jax.sharding.Mesh(parts, SEG_PARTS + EXP_PARTS)
    rows_heads = P(SEG_PARTS, EXP_PARTS)
    in_specs = (rows_heads, rows_heads, rows_heads, P(EXP_PARTS, SEG_PARTS), P(EXP_PARTS), rows_heads)
    out_specs = (rows_heads, rows_heads, rows_heads, rows_heads)
    return jax.shard_map(body, mesh=split, in_specs=in_specs, out_specs=out_specs, check_vma=False)
```

```python
import jax
import jax.numpy as jnp
from jax import lax
from jax.sharding import PartitionSpec as P

BLK = 512
EXP_PARTS = ("exp_y", "exp_x", "exp_core")
SEG_PARTS = ("seg_hi", "seg_lo")


EPS = 1e-06


def fade_weights(order, valid, logs, limit, extra=0.0):
    between = order & limit
    summed = jnp.sum(jnp.where(between[:, :, None], logs[None, :, :], 0.0), axis=1) + extra
    return jnp.where(valid[:, None], jnp.exp(summed), 0.0)


def mm(a, b):
    return lax.dot_general(a, b, (((1,), (0,)), ((), ())), preferred_element_type=jnp.float32)


def mm_t(a, b):
    return lax.dot_general(a, b, (((1,), (1,)), ((), ())), preferred_element_type=jnp.float32)


def tm(a, b):
    return lax.dot_general(a, b, (((0,), (0,)), ((), ())), preferred_element_type=jnp.float32)


def body(queries, keys, values, log_decay, gain, d_out):
    rows, width = queries.shape
    local_heads = log_decay.shape[0]
    head_width = width // local_heads
    count = rows // BLK
    pairs = [(block, head) for block in range(count) for head in range(local_heads)]
    place = jnp.arange(BLK)
    lower = place[:, None] >= place[None, :]

    def tile(array, block, head):
        return array[block * BLK:(block + 1) * BLK, head * head_width:(head + 1) * head_width]

    q, k, v, up, mask, grow, shrink, scores = {}, {}, {}, {}, {}, {}, {}, {}
    block_state, block_fade = {}, {}
    for block, head in pairs:
        key = (block, head)
        q[key] = tile(queries, block, head)
        k[key] = tile(keys, block, head)
        v[key] = tile(values, block, head)
        up[key] = tile(d_out, block, head).astype(jnp.float32)
        cumulative = jnp.cumsum(log_decay[head, block * BLK:(block + 1) * BLK])
        total = cumulative[-1]
        spread = cumulative[:, None] - cumulative[None, :]
        mask[key] = jnp.where(lower, jnp.exp(jnp.minimum(spread, 0.0)), 0.0)
        grow[key] = jnp.exp(cumulative)[:, None]
        shrink[key] = jnp.exp(total - cumulative)[:, None]
        block_fade[key] = jnp.exp(total)
        scores[key] = (mm_t(q[key], k[key]) * mask[key]).astype(jnp.bfloat16)
        key_weighted = (k[key] * shrink[key]).astype(jnp.bfloat16)
        block_state[key] = tm(key_weighted, v[key])
    fades = [jnp.stack([block_fade[(block, head)] for head in range(local_heads)]) for block in range(count)]
    states = [jnp.stack([block_state[(block, head)] for head in range(local_heads)]) for block in range(count)]
    seg_state = states[0]
    for block in range(1, count):
        seg_state = fades[block][:, None, None] * seg_state + states[block]
    low = lax.axis_index("seg_lo")
    high = lax.axis_index("seg_hi")
    low_places = jnp.arange(lax.axis_size("seg_lo"))
    high_places = jnp.arange(lax.axis_size("seg_hi"))
    seg_log = jnp.sum(log_decay, axis=-1)
    log_rows = jnp.broadcast_to(seg_log[:, None, None], (local_heads, 8, head_width))
    first = lax.all_gather(jnp.concatenate((seg_state, log_rows), axis=1), "seg_lo")
    low_states = first[:, :, :head_width, :]
    low_logs = first[:, :, head_width, 0]
    inside = fade_weights(low_places[:, None] < low_places[None, :], low_places < low, low_logs, low_places[None, :] < low)
    within = jnp.sum(inside[:, :, None, None] * low_states, axis=0)
    to_end = fade_weights(low_places[:, None] < low_places[None, :], low_places >= 0, low_logs, True)
    group_state = jnp.sum(to_end[:, :, None, None] * low_states, axis=0)
    group_log = jnp.sum(low_logs, axis=0)
    group_rows = jnp.broadcast_to(group_log[:, None, None], (local_heads, 8, head_width))
    second = lax.all_gather(jnp.concatenate((group_state, group_rows), axis=1), "seg_hi")
    high_states = second[:, :, :head_width, :]
    high_logs = second[:, :, head_width, 0]
    before_here = jnp.sum(jnp.where((low_places < low)[:, None], low_logs, 0.0), axis=0)
    outside = fade_weights(
        high_places[:, None] < high_places[None, :], high_places < high, high_logs, high_places[None, :] < high, before_here
    )
    running = within + jnp.sum(outside[:, :, None, None] * high_states, axis=0)
    held, attended = {}, {}
    for block in range(count):
        for head in range(local_heads):
            held[(block, head)] = running[head].astype(jnp.bfloat16)
        running = fades[block][:, None, None] * running + states[block]
    squares, cross = [], []
    for block in range(count):
        square_sum, cross_sum = 0.0, 0.0
        for head in range(local_heads):
            key = (block, head)
            inner = mm(scores[key], v[key])
            attended[key] = inner + grow[key] * mm(q[key], held[key])
            gain_here = gain[head * head_width:(head + 1) * head_width]
            square_sum = square_sum + jnp.sum(attended[key] * attended[key], axis=-1)
            cross_sum = cross_sum + jnp.sum(gain_here * up[key] * attended[key], axis=-1)
        squares.append(square_sum)
        cross.append(cross_sum)
    partial = jnp.stack((jnp.concatenate(squares), jnp.concatenate(cross)))
    totals_exp = partial
    for axis in EXP_PARTS[::-1]:
        totals_exp = lax.psum(totals_exp, axis)
    features = width * lax.axis_size(EXP_PARTS)
    outs, grads, back_terms = {}, {}, {}
    for block, head in pairs:
        key = (block, head)
        rows_here = slice(block * BLK, (block + 1) * BLK)
        inv_rms = lax.rsqrt(totals_exp[0, rows_here] / features + EPS)[:, None]
        cross_here = totals_exp[1, rows_here][:, None]
        gain_here = gain[head * head_width:(head + 1) * head_width]
        outs[key] = (attended[key] * inv_rms * gain_here).astype(jnp.bfloat16)
        grads[key] = (
            gain_here * up[key] * inv_rms
            - attended[key] * inv_rms * inv_rms * inv_rms * cross_here / features
        ).astype(jnp.bfloat16)
        query_weighted = (q[key] * grow[key]).astype(jnp.bfloat16)
        back_terms[key] = tm(query_weighted, grads[key])
    backs = [jnp.stack([back_terms[(block, head)] for head in range(local_heads)]) for block in range(count)]
    seg_back = backs[count - 1]
    for block in range(count - 2, -1, -1):
        seg_back = backs[block] + fades[block][:, None, None] * seg_back
    third = lax.all_gather(seg_back, "seg_lo")
    inside_back = fade_weights(low_places[:, None] > low_places[None, :], low_places > low, low_logs, low_places[None, :] > low)
    within_back = jnp.sum(inside_back[:, :, None, None] * third, axis=0)
    to_start = fade_weights(low_places[:, None] > low_places[None, :], low_places >= 0, low_logs, True)
    group_back = jnp.sum(to_start[:, :, None, None] * third, axis=0)
    fourth = lax.all_gather(group_back, "seg_hi")
    after_here = jnp.sum(jnp.where((low_places > low)[:, None], low_logs, 0.0), axis=0)
    outside_back = fade_weights(
        high_places[:, None] > high_places[None, :], high_places > high, high_logs, high_places[None, :] > high, after_here
    )
    running = within_back + jnp.sum(outside_back[:, :, None, None] * fourth, axis=0)
    exits = {}
    for block in range(count - 1, -1, -1):
        for head in range(local_heads):
            exits[(block, head)] = running[head].astype(jnp.bfloat16)
        running = backs[block] + fades[block][:, None, None] * running
    grad_q, grad_k, grad_v = {}, {}, {}
    for block, head in pairs:
        key = (block, head)
        grad_scores = (mm_t(grads[key], v[key]) * mask[key]).astype(jnp.bfloat16)
        grad_q[key] = (mm(grad_scores, k[key]) + grow[key] * mm_t(grads[key], held[key])).astype(jnp.bfloat16)
        grad_k[key] = (tm(grad_scores, q[key]) + shrink[key] * mm_t(v[key], exits[key])).astype(jnp.bfloat16)
        grad_v[key] = (tm(scores[key], grads[key]) + shrink[key] * mm(k[key], exits[key])).astype(jnp.bfloat16)

    def whole(parts):
        return jnp.concatenate(
            [jnp.concatenate([parts[(block, head)] for head in range(local_heads)], axis=1) for block in range(count)],
            axis=0,
        )

    return whole(outs), whole(grad_q), whole(grad_k), whole(grad_v)


def solution(mesh):
    parts = mesh.devices.reshape(4, -1, 4, mesh.devices.shape[1] // 8, 2)
    split = jax.sharding.Mesh(parts, SEG_PARTS + EXP_PARTS)
    rows_heads = P(SEG_PARTS, EXP_PARTS)
    in_specs = (rows_heads, rows_heads, rows_heads, P(EXP_PARTS, SEG_PARTS), P(EXP_PARTS), rows_heads)
    out_specs = (rows_heads, rows_heads, rows_heads, rows_heads)
    return jax.shard_map(body, mesh=split, in_specs=in_specs, out_specs=out_specs, check_vma=False)
```

```python
import jax
import jax.numpy as jnp
from jax import lax
from jax.sharding import PartitionSpec as P

BLK = 512
EXP_PARTS = ("exp_y", "exp_x", "exp_core")
SEG_PARTS = ("seg_hi", "seg_mid", "seg_lo")


EPS = 1e-06


def decay_parts(log_block):
    cumulative = jnp.cumsum(log_block, axis=-1)
    length = log_block.shape[-1]
    spread = cumulative[..., :, None] - cumulative[..., None, :]
    token_place = jnp.arange(length)
    lower = token_place[:, None] >= token_place[None, :]
    mask = jnp.where(lower, jnp.exp(jnp.minimum(spread, 0.0)), 0.0)
    return (cumulative, cumulative[..., -1], mask)


def fade_weights(order, valid, logs, limit, extra=0.0):
    between = order & limit
    summed = jnp.sum(jnp.where(between[:, :, None], logs[None, :, :], 0.0), axis=1) + extra
    return jnp.where(valid[:, None], jnp.exp(summed), 0.0)


def body(queries, keys, values, log_decay, gain, d_out):
    rows, width = queries.shape
    local_heads = log_decay.shape[0]
    head_width = width // local_heads
    count = rows // BLK
    shape = (count, BLK, local_heads, head_width)
    qblocks = queries.reshape(shape)
    kblocks = keys.reshape(shape)
    vblocks = values.reshape(shape)
    lblocks = log_decay.reshape(local_heads, count, BLK).transpose(1, 0, 2)
    cumulative, totals, mask = decay_parts(lblocks)
    grow = jnp.exp(cumulative).transpose(0, 2, 1)[..., None]
    shrink = jnp.exp(totals[:, None, :] - cumulative.transpose(0, 2, 1))[..., None]
    scores = (
        jnp.einsum("bthe,bshe->bhts", qblocks, kblocks, preferred_element_type=jnp.float32) * mask
    ).astype(jnp.bfloat16)
    inner = jnp.einsum("bhts,bshf->bthf", scores, vblocks, preferred_element_type=jnp.float32)
    key_weighted = (kblocks * shrink).astype(jnp.bfloat16)
    block_state = jnp.einsum(
        "bshe,bshf->bhef", key_weighted, vblocks, preferred_element_type=jnp.float32
    )
    block_fade = jnp.exp(totals)
    seg_state = block_state[0]
    for block in range(1, count):
        seg_state = block_fade[block][:, None, None] * seg_state + block_state[block]
    seg_log = jnp.sum(log_decay, axis=-1)
    level_logs = []
    level_here = []
    entering = jnp.zeros_like(seg_state)
    offset = jnp.zeros_like(seg_log)
    unit_state, unit_log = seg_state, seg_log
    for axis in SEG_PARTS[::-1]:
        here = lax.axis_index(axis)
        places = jnp.arange(lax.axis_size(axis))
        log_rows = jnp.broadcast_to(unit_log[:, None, None], (local_heads, 8, head_width))
        gathered = lax.all_gather(jnp.concatenate((unit_state, log_rows), axis=1), axis)
        states = gathered[:, :, :head_width, :]
        logs = gathered[:, :, head_width, 0]
        level_logs.append(logs)
        level_here.append(here)
        inside = fade_weights(places[:, None] < places[None, :], places < here, logs, places[None, :] < here, offset)
        entering = entering + jnp.sum(inside[:, :, None, None] * states, axis=0)
        offset = offset + jnp.sum(jnp.where((places < here)[:, None], logs, 0.0), axis=0)
        to_end = fade_weights(places[:, None] < places[None, :], places >= 0, logs, True)
        unit_state = jnp.sum(to_end[:, :, None, None] * states, axis=0)
        unit_log = jnp.sum(logs, axis=0)
    held_list = []
    running = entering
    for block in range(count):
        held_list.append(running.astype(jnp.bfloat16))
        running = block_fade[block][:, None, None] * running + block_state[block]
    held = jnp.stack(held_list)
    attended = inner + grow * jnp.einsum(
        "bthe,bhef->bthf", qblocks, held, preferred_element_type=jnp.float32
    )
    attended = attended.reshape(rows, width)
    upstream = d_out.astype(jnp.float32)
    partial = jnp.stack(
        (jnp.sum(attended * attended, axis=-1), jnp.sum(gain * upstream * attended, axis=-1))
    )
    totals_exp = partial
    for axis in EXP_PARTS[::-1]:
        totals_exp = lax.psum(totals_exp, axis)
    squares, cross = totals_exp[0], totals_exp[1]
    features = width * lax.axis_size(EXP_PARTS)
    inv_rms = lax.rsqrt(squares / features + EPS)[:, None]
    out = (attended * inv_rms * gain).astype(jnp.bfloat16)
    grad_attended = (
        gain * upstream * inv_rms
        - attended * inv_rms * inv_rms * inv_rms * cross[:, None] / features
    ).astype(jnp.bfloat16)
    grad_blocks = grad_attended.reshape(shape)
    query_weighted = (qblocks * grow).astype(jnp.bfloat16)
    back_terms = jnp.einsum(
        "bthe,bthf->bhef", query_weighted, grad_blocks, preferred_element_type=jnp.float32
    )
    seg_back = back_terms[count - 1]
    for block in range(count - 2, -1, -1):
        seg_back = back_terms[block] + block_fade[block][:, None, None] * seg_back
    leaving = jnp.zeros_like(seg_back)
    offset = jnp.zeros_like(seg_log)
    unit_back = seg_back
    for axis, logs, here in zip(SEG_PARTS[::-1], level_logs, level_here):
        places = jnp.arange(lax.axis_size(axis))
        backs = lax.all_gather(unit_back, axis)
        inside = fade_weights(places[:, None] > places[None, :], places > here, logs, places[None, :] > here, offset)
        leaving = leaving + jnp.sum(inside[:, :, None, None] * backs, axis=0)
        offset = offset + jnp.sum(jnp.where((places > here)[:, None], logs, 0.0), axis=0)
        to_start = fade_weights(places[:, None] > places[None, :], places >= 0, logs, True)
        unit_back = jnp.sum(to_start[:, :, None, None] * backs, axis=0)
    exit_list = [None] * count
    running = leaving
    for block in range(count - 1, -1, -1):
        exit_list[block] = running.astype(jnp.bfloat16)
        running = back_terms[block] + block_fade[block][:, None, None] * running
    exits = jnp.stack(exit_list)
    grad_scores = (
        jnp.einsum("bthf,bshf->bhts", grad_blocks, vblocks, preferred_element_type=jnp.float32)
        * mask
    ).astype(jnp.bfloat16)
    grad_q = jnp.einsum("bhts,bshe->bthe", grad_scores, kblocks, preferred_element_type=jnp.float32)
    grad_q = grad_q + grow * jnp.einsum(
        "bthf,bhef->bthe", grad_blocks, held, preferred_element_type=jnp.float32
    )
    grad_k = jnp.einsum("bhts,bthe->bshe", grad_scores, qblocks, preferred_element_type=jnp.float32)
    grad_k = grad_k + shrink * jnp.einsum(
        "bshf,bhef->bshe", vblocks, exits, preferred_element_type=jnp.float32
    )
    grad_v = jnp.einsum("bhts,bthf->bshf", scores, grad_blocks, preferred_element_type=jnp.float32)
    grad_v = grad_v + shrink * jnp.einsum(
        "bshe,bhef->bshf", kblocks, exits, preferred_element_type=jnp.float32
    )
    return (
        out,
        grad_q.reshape(rows, width).astype(jnp.bfloat16),
        grad_k.reshape(rows, width).astype(jnp.bfloat16),
        grad_v.reshape(rows, width).astype(jnp.bfloat16),
    )


def solution(mesh):
    parts = mesh.devices.reshape(2, 2, -1, 4, mesh.devices.shape[1] // 8, 2)
    split = jax.sharding.Mesh(parts, SEG_PARTS + EXP_PARTS)
    rows_heads = P(SEG_PARTS, EXP_PARTS)
    in_specs = (rows_heads, rows_heads, rows_heads, P(EXP_PARTS, SEG_PARTS), P(EXP_PARTS), rows_heads)
    out_specs = (rows_heads, rows_heads, rows_heads, rows_heads)
    return jax.shard_map(body, mesh=split, in_specs=in_specs, out_specs=out_specs, check_vma=False)
```

```python
import jax
import jax.numpy as jnp
from jax import lax
from jax.sharding import PartitionSpec as P

BLK = 512
EXP_PARTS = ("exp_y", "exp_x", "exp_core")
SEG_PARTS = ("seg_hi", "seg_lo")


EPS = 1e-06


def decay_parts(log_block):
    cumulative = jnp.cumsum(log_block, axis=-1)
    length = log_block.shape[-1]
    spread = cumulative[..., :, None] - cumulative[..., None, :]
    token_place = jnp.arange(length)
    lower = token_place[:, None] >= token_place[None, :]
    mask = jnp.where(lower, jnp.exp(jnp.minimum(spread, 0.0)), 0.0)
    return (cumulative, cumulative[..., -1], mask)


def fade_weights(order, valid, logs, limit, extra=0.0):
    between = order & limit
    summed = jnp.sum(jnp.where(between[:, :, None], logs[None, :, :], 0.0), axis=1) + extra
    return jnp.where(valid[:, None], jnp.exp(summed), 0.0)


def body(queries, keys, values, log_decay, gain, d_out):
    rows, width = queries.shape
    local_heads = log_decay.shape[0]
    head_width = width // local_heads
    count = rows // BLK
    view = (count, BLK, width)
    lblocks = log_decay.reshape(local_heads, count, BLK).transpose(1, 0, 2)
    cumulative, totals, mask = decay_parts(lblocks)
    qv, kv, vv, uv = (a.reshape(view) for a in (queries, keys, values, d_out))
    cols = [slice(head * head_width, (head + 1) * head_width) for head in range(local_heads)]
    qh = [qv[:, :, c] for c in cols]
    kh = [kv[:, :, c] for c in cols]
    vh = [vv[:, :, c] for c in cols]
    grow = [jnp.exp(cumulative[:, head, :])[..., None] for head in range(local_heads)]
    shrink = [jnp.exp(totals[:, head, None] - cumulative[:, head, :])[..., None] for head in range(local_heads)]
    scores = [
        (jnp.einsum("bte,bse->bts", qh[h], kh[h], preferred_element_type=jnp.float32) * mask[:, h]).astype(jnp.bfloat16)
        for h in range(local_heads)
    ]
    inner = [jnp.einsum("bts,bsf->btf", scores[h], vh[h], preferred_element_type=jnp.float32) for h in range(local_heads)]
    block_state = jnp.stack(
        [
            jnp.einsum("bse,bsf->bef", (kh[h] * shrink[h]).astype(jnp.bfloat16), vh[h], preferred_element_type=jnp.float32)
            for h in range(local_heads)
        ],
        axis=1,
    )
    block_fade = jnp.exp(totals)
    seg_state = block_state[0]
    for block in range(1, count):
        seg_state = block_fade[block][:, None, None] * seg_state + block_state[block]
    low = lax.axis_index("seg_lo")
    high = lax.axis_index("seg_hi")
    low_places = jnp.arange(lax.axis_size("seg_lo"))
    high_places = jnp.arange(lax.axis_size("seg_hi"))
    seg_log = jnp.sum(log_decay, axis=-1)
    log_rows = jnp.broadcast_to(seg_log[:, None, None], (local_heads, 8, head_width))
    first = lax.all_gather(jnp.concatenate((seg_state, log_rows), axis=1), "seg_lo")
    low_states = first[:, :, :head_width, :]
    low_logs = first[:, :, head_width, 0]
    inside = fade_weights(low_places[:, None] < low_places[None, :], low_places < low, low_logs, low_places[None, :] < low)
    within = jnp.sum(inside[:, :, None, None] * low_states, axis=0)
    to_end = fade_weights(low_places[:, None] < low_places[None, :], low_places >= 0, low_logs, True)
    group_state = jnp.sum(to_end[:, :, None, None] * low_states, axis=0)
    group_log = jnp.sum(low_logs, axis=0)
    group_rows = jnp.broadcast_to(group_log[:, None, None], (local_heads, 8, head_width))
    second = lax.all_gather(jnp.concatenate((group_state, group_rows), axis=1), "seg_hi")
    high_states = second[:, :, :head_width, :]
    high_logs = second[:, :, head_width, 0]
    before_here = jnp.sum(jnp.where((low_places < low)[:, None], low_logs, 0.0), axis=0)
    outside = fade_weights(
        high_places[:, None] < high_places[None, :], high_places < high, high_logs, high_places[None, :] < high, before_here
    )
    entering = within + jnp.sum(outside[:, :, None, None] * high_states, axis=0)
    held_list = []
    running = entering
    for block in range(count):
        held_list.append(running.astype(jnp.bfloat16))
        running = block_fade[block][:, None, None] * running + block_state[block]
    held = jnp.stack(held_list)
    attended = jnp.concatenate(
        [
            inner[h] + grow[h] * jnp.einsum("bte,bef->btf", qh[h], held[:, h], preferred_element_type=jnp.float32)
            for h in range(local_heads)
        ],
        axis=-1,
    ).reshape(rows, width)
    upstream = d_out.astype(jnp.float32)
    partial = jnp.stack(
        (jnp.sum(attended * attended, axis=-1), jnp.sum(gain * upstream * attended, axis=-1))
    )
    totals_exp = partial
    for axis in EXP_PARTS[::-1]:
        totals_exp = lax.psum(totals_exp, axis)
    squares, cross = totals_exp[0], totals_exp[1]
    features = width * lax.axis_size(EXP_PARTS)
    inv_rms = lax.rsqrt(squares / features + EPS)[:, None]
    out = (attended * inv_rms * gain).astype(jnp.bfloat16)
    grad_attended = (
        gain * upstream * inv_rms
        - attended * inv_rms * inv_rms * inv_rms * cross[:, None] / features
    ).astype(jnp.bfloat16)
    gv = grad_attended.reshape(view)
    gh = [gv[:, :, c] for c in cols]
    back_terms = jnp.stack(
        [
            jnp.einsum("bte,btf->bef", (qh[h] * grow[h]).astype(jnp.bfloat16), gh[h], preferred_element_type=jnp.float32)
            for h in range(local_heads)
        ],
        axis=1,
    )
    seg_back = back_terms[count - 1]
    for block in range(count - 2, -1, -1):
        seg_back = back_terms[block] + block_fade[block][:, None, None] * seg_back
    third = lax.all_gather(seg_back, "seg_lo")
    inside_back = fade_weights(low_places[:, None] > low_places[None, :], low_places > low, low_logs, low_places[None, :] > low)
    within_back = jnp.sum(inside_back[:, :, None, None] * third, axis=0)
    to_start = fade_weights(low_places[:, None] > low_places[None, :], low_places >= 0, low_logs, True)
    group_back = jnp.sum(to_start[:, :, None, None] * third, axis=0)
    fourth = lax.all_gather(group_back, "seg_hi")
    after_here = jnp.sum(jnp.where((low_places > low)[:, None], low_logs, 0.0), axis=0)
    outside_back = fade_weights(
        high_places[:, None] > high_places[None, :], high_places > high, high_logs, high_places[None, :] > high, after_here
    )
    leaving = within_back + jnp.sum(outside_back[:, :, None, None] * fourth, axis=0)
    exit_list = [None] * count
    running = leaving
    for block in range(count - 1, -1, -1):
        exit_list[block] = running.astype(jnp.bfloat16)
        running = back_terms[block] + block_fade[block][:, None, None] * running
    exits = jnp.stack(exit_list)
    grad_q, grad_k, grad_v = [], [], []
    for h in range(local_heads):
        grad_scores = (
            jnp.einsum("btf,bsf->bts", gh[h], vh[h], preferred_element_type=jnp.float32) * mask[:, h]
        ).astype(jnp.bfloat16)
        gq = jnp.einsum("bts,bse->bte", grad_scores, kh[h], preferred_element_type=jnp.float32)
        gq = gq + grow[h] * jnp.einsum("btf,bef->bte", gh[h], held[:, h], preferred_element_type=jnp.float32)
        gk = jnp.einsum("bts,bte->bse", grad_scores, qh[h], preferred_element_type=jnp.float32)
        gk = gk + shrink[h] * jnp.einsum("bsf,bef->bse", vh[h], exits[:, h], preferred_element_type=jnp.float32)
        gvv = jnp.einsum("bts,btf->bsf", scores[h], gh[h], preferred_element_type=jnp.float32)
        gvv = gvv + shrink[h] * jnp.einsum("bse,bef->bsf", kh[h], exits[:, h], preferred_element_type=jnp.float32)
        grad_q.append(gq.astype(jnp.bfloat16))
        grad_k.append(gk.astype(jnp.bfloat16))
        grad_v.append(gvv.astype(jnp.bfloat16))

    def whole(parts):
        return jnp.concatenate(parts, axis=-1).reshape(rows, width)

    return out, whole(grad_q), whole(grad_k), whole(grad_v)


def solution(mesh):
    parts = mesh.devices.reshape(4, -1, 4, mesh.devices.shape[1] // 8, 2)
    split = jax.sharding.Mesh(parts, SEG_PARTS + EXP_PARTS)
    rows_heads = P(SEG_PARTS, EXP_PARTS)
    in_specs = (rows_heads, rows_heads, rows_heads, P(EXP_PARTS, SEG_PARTS), P(EXP_PARTS), rows_heads)
    out_specs = (rows_heads, rows_heads, rows_heads, rows_heads)
    return jax.shard_map(body, mesh=split, in_specs=in_specs, out_specs=out_specs, check_vma=False)
```

```python
import jax
import jax.numpy as jnp
from jax import lax
from jax.sharding import PartitionSpec as P

BLK = 512
EXP_PARTS = ("exp_y", "exp_x", "exp_core")
SEG_PARTS = ("seg_hi", "seg_lo")


EPS = 1e-06


def decay_parts(log_block):
    cumulative = jnp.cumsum(log_block, axis=-1)
    length = log_block.shape[-1]
    spread = cumulative[..., :, None] - cumulative[..., None, :]
    token_place = jnp.arange(length)
    lower = token_place[:, None] >= token_place[None, :]
    mask = jnp.where(lower, jnp.exp(jnp.minimum(spread, 0.0)), 0.0)
    return (cumulative, cumulative[..., -1], mask)


def fade_weights(order, valid, logs, limit, extra=0.0):
    between = order & limit
    summed = jnp.sum(jnp.where(between[:, :, None], logs[None, :, :], 0.0), axis=1) + extra
    return jnp.where(valid[:, None], jnp.exp(summed), 0.0)


def body(queries, keys, values, log_decay, gain, d_out):
    rows, width = queries.shape
    local_heads = log_decay.shape[0]
    head_width = width // local_heads
    count = rows // BLK
    view = (count, BLK, width)
    lblocks = log_decay.reshape(local_heads, count, BLK).transpose(1, 0, 2)
    cumulative, totals, mask = decay_parts(lblocks)
    qv, kv, vv, uv = (a.reshape(view) for a in (queries, keys, values, d_out))
    cols = [slice(head * head_width, (head + 1) * head_width) for head in range(local_heads)]
    qh = [qv[:, :, c] for c in cols]
    kh = [kv[:, :, c] for c in cols]
    vh = [vv[:, :, c] for c in cols]
    grow = [jnp.exp(cumulative[:, head, :])[..., None] for head in range(local_heads)]
    shrink = [jnp.exp(totals[:, head, None] - cumulative[:, head, :])[..., None] for head in range(local_heads)]
    scores = [
        (jnp.einsum("bte,bse->bts", qh[h], kh[h], preferred_element_type=jnp.float32) * mask[:, h]).astype(jnp.bfloat16)
        for h in range(local_heads)
    ]
    inner = [jnp.einsum("bts,bsf->btf", scores[h], vh[h], preferred_element_type=jnp.float32) for h in range(local_heads)]
    block_state = jnp.stack(
        [
            jnp.einsum("bse,bsf->bef", (kh[h] * shrink[h]).astype(jnp.bfloat16), vh[h], preferred_element_type=jnp.float32)
            for h in range(local_heads)
        ],
        axis=1,
    )
    block_fade = jnp.exp(totals)
    seg_state = block_state[0]
    for block in range(1, count):
        seg_state = block_fade[block][:, None, None] * seg_state + block_state[block]
    low = lax.axis_index("seg_lo")
    high = lax.axis_index("seg_hi")
    low_places = jnp.arange(lax.axis_size("seg_lo"))
    high_places = jnp.arange(lax.axis_size("seg_hi"))
    seg_log = jnp.sum(log_decay, axis=-1)
    log_rows = jnp.broadcast_to(seg_log[:, None, None], (local_heads, 8, head_width))
    first = lax.all_gather(jnp.concatenate((seg_state, log_rows), axis=1), "seg_lo")
    low_states = first[:, :, :head_width, :]
    low_logs = first[:, :, head_width, 0]
    inside = fade_weights(low_places[:, None] < low_places[None, :], low_places < low, low_logs, low_places[None, :] < low)
    within = jnp.sum(inside[:, :, None, None] * low_states, axis=0)
    to_end = fade_weights(low_places[:, None] < low_places[None, :], low_places >= 0, low_logs, True)
    group_state = jnp.sum(to_end[:, :, None, None] * low_states, axis=0)
    group_log = jnp.sum(low_logs, axis=0)
    share = head_width // lax.axis_size("seg_lo")
    group_rows = jnp.broadcast_to(group_log[:, None, None], (local_heads, 8, head_width))
    quarter = lax.dynamic_slice_in_dim(group_state, low * share, share, axis=1)
    second = lax.all_gather(jnp.concatenate((quarter, group_rows), axis=1), "seg_hi")
    high_states = second[:, :, :share, :]
    high_logs = second[:, :, share, 0]
    before_here = jnp.sum(jnp.where((low_places < low)[:, None], low_logs, 0.0), axis=0)
    outside = fade_weights(high_places[:, None] < high_places[None, :], high_places < high, high_logs, high_places[None, :] < high)
    carried = jnp.sum(outside[:, :, None, None] * high_states, axis=0)
    carried = lax.all_gather(carried, "seg_lo", axis=1, tiled=True)
    entering = within + jnp.exp(before_here)[:, None, None] * carried
    held_list = []
    running = entering
    for block in range(count):
        held_list.append(running.astype(jnp.bfloat16))
        running = block_fade[block][:, None, None] * running + block_state[block]
    held = jnp.stack(held_list)
    attended = jnp.concatenate(
        [
            inner[h] + grow[h] * jnp.einsum("bte,bef->btf", qh[h], held[:, h], preferred_element_type=jnp.float32)
            for h in range(local_heads)
        ],
        axis=-1,
    ).reshape(rows, width)
    upstream = d_out.astype(jnp.float32)
    partial = jnp.stack(
        (jnp.sum(attended * attended, axis=-1), jnp.sum(gain * upstream * attended, axis=-1))
    )
    totals_exp = partial
    for axis in EXP_PARTS[::-1]:
        totals_exp = lax.psum(totals_exp, axis)
    squares, cross = totals_exp[0], totals_exp[1]
    features = width * lax.axis_size(EXP_PARTS)
    inv_rms = lax.rsqrt(squares / features + EPS)[:, None]
    out = (attended * inv_rms * gain).astype(jnp.bfloat16)
    grad_attended = (
        gain * upstream * inv_rms
        - attended * inv_rms * inv_rms * inv_rms * cross[:, None] / features
    ).astype(jnp.bfloat16)
    gv = grad_attended.reshape(view)
    gh = [gv[:, :, c] for c in cols]
    back_terms = jnp.stack(
        [
            jnp.einsum("bte,btf->bef", (qh[h] * grow[h]).astype(jnp.bfloat16), gh[h], preferred_element_type=jnp.float32)
            for h in range(local_heads)
        ],
        axis=1,
    )
    seg_back = back_terms[count - 1]
    for block in range(count - 2, -1, -1):
        seg_back = back_terms[block] + block_fade[block][:, None, None] * seg_back
    third = lax.all_gather(seg_back, "seg_lo")
    inside_back = fade_weights(low_places[:, None] > low_places[None, :], low_places > low, low_logs, low_places[None, :] > low)
    within_back = jnp.sum(inside_back[:, :, None, None] * third, axis=0)
    to_start = fade_weights(low_places[:, None] > low_places[None, :], low_places >= 0, low_logs, True)
    group_back = jnp.sum(to_start[:, :, None, None] * third, axis=0)
    fourth = lax.all_gather(lax.dynamic_slice_in_dim(group_back, low * share, share, axis=1), "seg_hi")
    after_here = jnp.sum(jnp.where((low_places > low)[:, None], low_logs, 0.0), axis=0)
    outside_back = fade_weights(high_places[:, None] > high_places[None, :], high_places > high, high_logs, high_places[None, :] > high)
    carried_back = jnp.sum(outside_back[:, :, None, None] * fourth, axis=0)
    carried_back = lax.all_gather(carried_back, "seg_lo", axis=1, tiled=True)
    leaving = within_back + jnp.exp(after_here)[:, None, None] * carried_back
    exit_list = [None] * count
    running = leaving
    for block in range(count - 1, -1, -1):
        exit_list[block] = running.astype(jnp.bfloat16)
        running = back_terms[block] + block_fade[block][:, None, None] * running
    exits = jnp.stack(exit_list)
    grad_q, grad_k, grad_v = [], [], []
    for h in range(local_heads):
        grad_scores = (
            jnp.einsum("btf,bsf->bts", gh[h], vh[h], preferred_element_type=jnp.float32) * mask[:, h]
        ).astype(jnp.bfloat16)
        gq = jnp.einsum("bts,bse->bte", grad_scores, kh[h], preferred_element_type=jnp.float32)
        gq = gq + grow[h] * jnp.einsum("btf,bef->bte", gh[h], held[:, h], preferred_element_type=jnp.float32)
        gk = jnp.einsum("bts,bte->bse", grad_scores, qh[h], preferred_element_type=jnp.float32)
        gk = gk + shrink[h] * jnp.einsum("bsf,bef->bse", vh[h], exits[:, h], preferred_element_type=jnp.float32)
        gvv = jnp.einsum("bts,btf->bsf", scores[h], gh[h], preferred_element_type=jnp.float32)
        gvv = gvv + shrink[h] * jnp.einsum("bse,bef->bsf", kh[h], exits[:, h], preferred_element_type=jnp.float32)
        grad_q.append(gq.astype(jnp.bfloat16))
        grad_k.append(gk.astype(jnp.bfloat16))
        grad_v.append(gvv.astype(jnp.bfloat16))

    def whole(parts):
        return jnp.concatenate(parts, axis=-1).reshape(rows, width)

    return out, whole(grad_q), whole(grad_k), whole(grad_v)


def solution(mesh):
    parts = mesh.devices.reshape(4, -1, 4, mesh.devices.shape[1] // 8, 2)
    split = jax.sharding.Mesh(parts, SEG_PARTS + EXP_PARTS)
    rows_heads = P(SEG_PARTS, EXP_PARTS)
    in_specs = (rows_heads, rows_heads, rows_heads, P(EXP_PARTS, SEG_PARTS), P(EXP_PARTS), rows_heads)
    out_specs = (rows_heads, rows_heads, rows_heads, rows_heads)
    return jax.shard_map(body, mesh=split, in_specs=in_specs, out_specs=out_specs, check_vma=False)
```

```python
import jax
import jax.numpy as jnp
from jax import lax
from jax.sharding import PartitionSpec as P

BLK = 512
EXP_PARTS = ("exp_y", "exp_x", "exp_core")
SEG_PARTS = ("seg_hi", "seg_lo")


EPS = 1e-06


def decay_parts(log_block):
    cumulative = jnp.cumsum(log_block, axis=-1)
    length = log_block.shape[-1]
    spread = cumulative[..., :, None] - cumulative[..., None, :]
    token_place = jnp.arange(length)
    lower = token_place[:, None] >= token_place[None, :]
    mask = jnp.where(lower, jnp.exp(jnp.minimum(spread, 0.0)), 0.0)
    return (cumulative, cumulative[..., -1], mask)


def fade_weights(order, valid, logs, limit, extra=0.0):
    between = order & limit
    summed = jnp.sum(jnp.where(between[:, :, None], logs[None, :, :], 0.0), axis=1) + extra
    return jnp.where(valid[:, None], jnp.exp(summed), 0.0)


def body(queries, keys, values, log_decay, gain, d_out):
    rows, width = queries.shape
    local_heads = log_decay.shape[0]
    head_width = width // local_heads
    count = rows // BLK
    view = (count, BLK, width)
    lblocks = log_decay.reshape(local_heads, count, BLK).transpose(1, 0, 2)
    cumulative, totals, mask = decay_parts(lblocks)
    qv, kv, vv, uv = (a.reshape(view) for a in (queries, keys, values, d_out))
    cols = [slice(head * head_width, (head + 1) * head_width) for head in range(local_heads)]
    qh = [qv[:, :, c] for c in cols]
    kh = [kv[:, :, c] for c in cols]
    vh = [vv[:, :, c] for c in cols]
    grow = [jnp.exp(cumulative[:, head, :])[..., None] for head in range(local_heads)]
    shrink = [jnp.exp(totals[:, head, None] - cumulative[:, head, :])[..., None] for head in range(local_heads)]
    scores = [
        (jnp.einsum("bte,bse->bts", qh[h], kh[h], preferred_element_type=jnp.float32) * mask[:, h]).astype(jnp.bfloat16)
        for h in range(local_heads)
    ]
    inner = [jnp.einsum("bts,bsf->btf", scores[h], vh[h], preferred_element_type=jnp.float32) for h in range(local_heads)]
    block_state = jnp.stack(
        [
            jnp.einsum("bse,bsf->bef", (kh[h] * shrink[h]).astype(jnp.bfloat16), vh[h], preferred_element_type=jnp.float32)
            for h in range(local_heads)
        ],
        axis=1,
    )
    block_fade = jnp.exp(totals)
    seg_state = block_state[0]
    for block in range(1, count):
        seg_state = block_fade[block][:, None, None] * seg_state + block_state[block]
    low = lax.axis_index("seg_lo")
    high = lax.axis_index("seg_hi")
    low_places = jnp.arange(lax.axis_size("seg_lo"))
    high_places = jnp.arange(lax.axis_size("seg_hi"))
    seg_log = jnp.sum(log_decay, axis=-1)
    log_rows = jnp.broadcast_to(seg_log[:, None, None], (local_heads, 8, head_width))
    first = lax.all_gather(jnp.concatenate((seg_state, log_rows), axis=1), "seg_lo")
    low_states = first[:, :, :head_width, :]
    low_logs = first[:, :, head_width, 0]
    inside = fade_weights(low_places[:, None] < low_places[None, :], low_places < low, low_logs, low_places[None, :] < low)
    within = jnp.sum(inside[:, :, None, None] * low_states, axis=0)
    to_end = fade_weights(low_places[:, None] < low_places[None, :], low_places >= 0, low_logs, True)
    group_state = jnp.sum(to_end[:, :, None, None] * low_states, axis=0)
    group_log = jnp.sum(low_logs, axis=0)
    group_rows = jnp.broadcast_to(group_log[:, None, None], (local_heads, 8, head_width))
    second = lax.all_gather(jnp.concatenate((group_state, group_rows), axis=1), "seg_hi")
    high_states = second[:, :, :head_width, :]
    high_logs = second[:, :, head_width, 0]
    before_here = jnp.sum(jnp.where((low_places < low)[:, None], low_logs, 0.0), axis=0)
    outside = fade_weights(
        high_places[:, None] < high_places[None, :], high_places < high, high_logs, high_places[None, :] < high, before_here
    )
    entering = within + jnp.sum(outside[:, :, None, None] * high_states, axis=0)
    held_list = []
    running = entering
    for block in range(count):
        held_list.append(running.astype(jnp.bfloat16))
        running = block_fade[block][:, None, None] * running + block_state[block]
    held = jnp.stack(held_list)
    attended = jnp.concatenate(
        [
            inner[h] + grow[h] * jnp.einsum("bte,bef->btf", qh[h], held[:, h], preferred_element_type=jnp.float32)
            for h in range(local_heads)
        ],
        axis=-1,
    ).reshape(rows, width)
    upstream = d_out.astype(jnp.float32)
    partial = jnp.stack(
        (jnp.sum(attended * attended, axis=-1), jnp.sum(gain * upstream * attended, axis=-1))
    )
    seg_index = lax.axis_index(SEG_PARTS)
    slots = jnp.zeros((lax.axis_size(SEG_PARTS),) + partial.shape, partial.dtype)
    slots = lax.dynamic_update_index_in_dim(slots, partial, seg_index, axis=0)
    totals_exp = lax.dynamic_index_in_dim(lax.psum(slots, SEG_PARTS + EXP_PARTS), seg_index, axis=0, keepdims=False)
    squares, cross = totals_exp[0], totals_exp[1]
    features = width * lax.axis_size(EXP_PARTS)
    inv_rms = lax.rsqrt(squares / features + EPS)[:, None]
    out = (attended * inv_rms * gain).astype(jnp.bfloat16)
    grad_attended = (
        gain * upstream * inv_rms
        - attended * inv_rms * inv_rms * inv_rms * cross[:, None] / features
    ).astype(jnp.bfloat16)
    gv = grad_attended.reshape(view)
    gh = [gv[:, :, c] for c in cols]
    back_terms = jnp.stack(
        [
            jnp.einsum("bte,btf->bef", (qh[h] * grow[h]).astype(jnp.bfloat16), gh[h], preferred_element_type=jnp.float32)
            for h in range(local_heads)
        ],
        axis=1,
    )
    seg_back = back_terms[count - 1]
    for block in range(count - 2, -1, -1):
        seg_back = back_terms[block] + block_fade[block][:, None, None] * seg_back
    third = lax.all_gather(seg_back, "seg_lo")
    inside_back = fade_weights(low_places[:, None] > low_places[None, :], low_places > low, low_logs, low_places[None, :] > low)
    within_back = jnp.sum(inside_back[:, :, None, None] * third, axis=0)
    to_start = fade_weights(low_places[:, None] > low_places[None, :], low_places >= 0, low_logs, True)
    group_back = jnp.sum(to_start[:, :, None, None] * third, axis=0)
    fourth = lax.all_gather(group_back, "seg_hi")
    after_here = jnp.sum(jnp.where((low_places > low)[:, None], low_logs, 0.0), axis=0)
    outside_back = fade_weights(
        high_places[:, None] > high_places[None, :], high_places > high, high_logs, high_places[None, :] > high, after_here
    )
    leaving = within_back + jnp.sum(outside_back[:, :, None, None] * fourth, axis=0)
    exit_list = [None] * count
    running = leaving
    for block in range(count - 1, -1, -1):
        exit_list[block] = running.astype(jnp.bfloat16)
        running = back_terms[block] + block_fade[block][:, None, None] * running
    exits = jnp.stack(exit_list)
    grad_q, grad_k, grad_v = [], [], []
    for h in range(local_heads):
        grad_scores = (
            jnp.einsum("btf,bsf->bts", gh[h], vh[h], preferred_element_type=jnp.float32) * mask[:, h]
        ).astype(jnp.bfloat16)
        gq = jnp.einsum("bts,bse->bte", grad_scores, kh[h], preferred_element_type=jnp.float32)
        gq = gq + grow[h] * jnp.einsum("btf,bef->bte", gh[h], held[:, h], preferred_element_type=jnp.float32)
        gk = jnp.einsum("bts,bte->bse", grad_scores, qh[h], preferred_element_type=jnp.float32)
        gk = gk + shrink[h] * jnp.einsum("bsf,bef->bse", vh[h], exits[:, h], preferred_element_type=jnp.float32)
        gvv = jnp.einsum("bts,btf->bsf", scores[h], gh[h], preferred_element_type=jnp.float32)
        gvv = gvv + shrink[h] * jnp.einsum("bse,bef->bsf", kh[h], exits[:, h], preferred_element_type=jnp.float32)
        grad_q.append(gq.astype(jnp.bfloat16))
        grad_k.append(gk.astype(jnp.bfloat16))
        grad_v.append(gvv.astype(jnp.bfloat16))

    def whole(parts):
        return jnp.concatenate(parts, axis=-1).reshape(rows, width)

    return out, whole(grad_q), whole(grad_k), whole(grad_v)


def solution(mesh):
    parts = mesh.devices.reshape(4, -1, 4, mesh.devices.shape[1] // 8, 2)
    split = jax.sharding.Mesh(parts, SEG_PARTS + EXP_PARTS)
    rows_heads = P(SEG_PARTS, EXP_PARTS)
    in_specs = (rows_heads, rows_heads, rows_heads, P(EXP_PARTS, SEG_PARTS), P(EXP_PARTS), rows_heads)
    out_specs = (rows_heads, rows_heads, rows_heads, rows_heads)
    return jax.shard_map(body, mesh=split, in_specs=in_specs, out_specs=out_specs, check_vma=False)
```

```python
import jax
import jax.numpy as jnp
from jax import lax
from jax.sharding import PartitionSpec as P

BLK = 512
EXP_PARTS = ("exp_y", "exp_x", "exp_core")
SEG_PARTS = ("seg_hi", "seg_lo")


EPS = 1e-06


def decay_parts(log_block):
    cumulative = jnp.cumsum(log_block, axis=-1)
    length = log_block.shape[-1]
    spread = cumulative[..., :, None] - cumulative[..., None, :]
    token_place = jnp.arange(length)
    lower = token_place[:, None] >= token_place[None, :]
    mask = jnp.where(lower, jnp.exp(jnp.minimum(spread, 0.0)), 0.0)
    return (cumulative, cumulative[..., -1], mask)


def fade_weights(order, valid, logs, limit, extra=0.0):
    between = order & limit
    summed = jnp.sum(jnp.where(between[:, :, None], logs[None, :, :], 0.0), axis=1) + extra
    return jnp.where(valid[:, None], jnp.exp(summed), 0.0)


def body(queries, keys, values, log_decay, gain, d_out):
    rows, width = queries.shape
    local_heads = log_decay.shape[0]
    head_width = width // local_heads
    count = rows // BLK
    view = (count, BLK, width)
    lblocks = log_decay.reshape(local_heads, count, BLK).transpose(1, 0, 2)
    cumulative, totals, mask = decay_parts(lblocks)
    qv, kv, vv, uv = (a.reshape(view) for a in (queries, keys, values, d_out))
    cols = [slice(head * head_width, (head + 1) * head_width) for head in range(local_heads)]
    qh = [qv[:, :, c] for c in cols]
    kh = [kv[:, :, c] for c in cols]
    vh = [vv[:, :, c] for c in cols]
    grow = [jnp.exp(cumulative[:, head, :])[..., None] for head in range(local_heads)]
    shrink = [jnp.exp(totals[:, head, None] - cumulative[:, head, :])[..., None] for head in range(local_heads)]
    scores = [
        (jnp.einsum("bte,bse->bts", qh[h], kh[h], preferred_element_type=jnp.float32) * mask[:, h]).astype(jnp.bfloat16)
        for h in range(local_heads)
    ]
    inner = [jnp.einsum("bts,bsf->btf", scores[h], vh[h], preferred_element_type=jnp.float32) for h in range(local_heads)]
    block_state = jnp.stack(
        [
            jnp.einsum("bse,bsf->bef", (kh[h] * shrink[h]).astype(jnp.bfloat16), vh[h], preferred_element_type=jnp.float32)
            for h in range(local_heads)
        ],
        axis=1,
    )
    block_fade = jnp.exp(totals)
    seg_state = block_state[0]
    for block in range(1, count):
        seg_state = block_fade[block][:, None, None] * seg_state + block_state[block]
    low = lax.axis_index("seg_lo")
    high = lax.axis_index("seg_hi")
    low_places = jnp.arange(lax.axis_size("seg_lo"))
    high_places = jnp.arange(lax.axis_size("seg_hi"))
    seg_log = jnp.sum(log_decay, axis=-1)
    log_rows = jnp.broadcast_to(seg_log[:, None, None], (local_heads, 8, head_width))
    first = lax.all_gather(jnp.concatenate((seg_state, log_rows), axis=1), "seg_lo")
    low_states = first[:, :, :head_width, :]
    low_logs = first[:, :, head_width, 0]
    inside = fade_weights(low_places[:, None] < low_places[None, :], low_places < low, low_logs, low_places[None, :] < low)
    within = jnp.sum(inside[:, :, None, None] * low_states, axis=0)
    to_end = fade_weights(low_places[:, None] < low_places[None, :], low_places >= 0, low_logs, True)
    group_state = jnp.sum(to_end[:, :, None, None] * low_states, axis=0)
    group_log = jnp.sum(low_logs, axis=0)
    group_rows = jnp.broadcast_to(group_log[:, None, None], (local_heads, 8, head_width))
    second = lax.all_gather(jnp.concatenate((group_state, group_rows), axis=1), "seg_hi")
    high_states = second[:, :, :head_width, :]
    high_logs = second[:, :, head_width, 0]
    before_here = jnp.sum(jnp.where((low_places < low)[:, None], low_logs, 0.0), axis=0)
    outside = fade_weights(
        high_places[:, None] < high_places[None, :], high_places < high, high_logs, high_places[None, :] < high, before_here
    )
    entering = within + jnp.sum(outside[:, :, None, None] * high_states, axis=0)
    held_list = []
    running = entering
    for block in range(count):
        held_list.append(running.astype(jnp.bfloat16))
        running = block_fade[block][:, None, None] * running + block_state[block]
    held = jnp.stack(held_list)
    gains = [gain[c] for c in cols]
    ups = [uv[:, :, c].astype(jnp.float32) for c in cols]
    attended = [
        inner[h] + grow[h] * jnp.einsum("bte,bef->btf", qh[h], held[:, h], preferred_element_type=jnp.float32)
        for h in range(local_heads)
    ]
    squares_local = sum(jnp.sum(attended[h] * attended[h], axis=-1) for h in range(local_heads))
    cross_local = sum(jnp.sum(gains[h] * ups[h] * attended[h], axis=-1) for h in range(local_heads))
    partial = jnp.stack((squares_local.reshape(rows), cross_local.reshape(rows)))
    totals_exp = partial
    for axis in EXP_PARTS[::-1]:
        totals_exp = lax.psum(totals_exp, axis)
    squares, cross = totals_exp[0].reshape(count, BLK), totals_exp[1].reshape(count, BLK)
    features = width * lax.axis_size(EXP_PARTS)
    inv_rms = lax.rsqrt(squares / features + EPS)[..., None]
    out = jnp.concatenate(
        [(attended[h] * inv_rms * gains[h]).astype(jnp.bfloat16) for h in range(local_heads)], axis=-1
    ).reshape(rows, width)
    gh = [
        (
            gains[h] * ups[h] * inv_rms
            - attended[h] * inv_rms * inv_rms * inv_rms * cross[..., None] / features
        ).astype(jnp.bfloat16)
        for h in range(local_heads)
    ]
    back_terms = jnp.stack(
        [
            jnp.einsum("bte,btf->bef", (qh[h] * grow[h]).astype(jnp.bfloat16), gh[h], preferred_element_type=jnp.float32)
            for h in range(local_heads)
        ],
        axis=1,
    )
    seg_back = back_terms[count - 1]
    for block in range(count - 2, -1, -1):
        seg_back = back_terms[block] + block_fade[block][:, None, None] * seg_back
    third = lax.all_gather(seg_back, "seg_lo")
    inside_back = fade_weights(low_places[:, None] > low_places[None, :], low_places > low, low_logs, low_places[None, :] > low)
    within_back = jnp.sum(inside_back[:, :, None, None] * third, axis=0)
    to_start = fade_weights(low_places[:, None] > low_places[None, :], low_places >= 0, low_logs, True)
    group_back = jnp.sum(to_start[:, :, None, None] * third, axis=0)
    fourth = lax.all_gather(group_back, "seg_hi")
    after_here = jnp.sum(jnp.where((low_places > low)[:, None], low_logs, 0.0), axis=0)
    outside_back = fade_weights(
        high_places[:, None] > high_places[None, :], high_places > high, high_logs, high_places[None, :] > high, after_here
    )
    leaving = within_back + jnp.sum(outside_back[:, :, None, None] * fourth, axis=0)
    exit_list = [None] * count
    running = leaving
    for block in range(count - 1, -1, -1):
        exit_list[block] = running.astype(jnp.bfloat16)
        running = back_terms[block] + block_fade[block][:, None, None] * running
    exits = jnp.stack(exit_list)
    grad_q, grad_k, grad_v = [], [], []
    for h in range(local_heads):
        grad_scores = (
            jnp.einsum("btf,bsf->bts", gh[h], vh[h], preferred_element_type=jnp.float32) * mask[:, h]
        ).astype(jnp.bfloat16)
        gq = jnp.einsum("bts,bse->bte", grad_scores, kh[h], preferred_element_type=jnp.float32)
        gq = gq + grow[h] * jnp.einsum("btf,bef->bte", gh[h], held[:, h], preferred_element_type=jnp.float32)
        gk = jnp.einsum("bts,bte->bse", grad_scores, qh[h], preferred_element_type=jnp.float32)
        gk = gk + shrink[h] * jnp.einsum("bsf,bef->bse", vh[h], exits[:, h], preferred_element_type=jnp.float32)
        gvv = jnp.einsum("bts,btf->bsf", scores[h], gh[h], preferred_element_type=jnp.float32)
        gvv = gvv + shrink[h] * jnp.einsum("bse,bef->bsf", kh[h], exits[:, h], preferred_element_type=jnp.float32)
        grad_q.append(gq.astype(jnp.bfloat16))
        grad_k.append(gk.astype(jnp.bfloat16))
        grad_v.append(gvv.astype(jnp.bfloat16))

    def whole(parts):
        return jnp.concatenate(parts, axis=-1).reshape(rows, width)

    return out, whole(grad_q), whole(grad_k), whole(grad_v)


def solution(mesh):
    parts = mesh.devices.reshape(4, -1, 4, mesh.devices.shape[1] // 8, 2)
    split = jax.sharding.Mesh(parts, SEG_PARTS + EXP_PARTS)
    rows_heads = P(SEG_PARTS, EXP_PARTS)
    in_specs = (rows_heads, rows_heads, rows_heads, P(EXP_PARTS, SEG_PARTS), P(EXP_PARTS), rows_heads)
    out_specs = (rows_heads, rows_heads, rows_heads, rows_heads)
    return jax.shard_map(body, mesh=split, in_specs=in_specs, out_specs=out_specs, check_vma=False)
```
